256 devices in a mesh: gx: 32 (over z, y_hi, core), gy: 8 (over y_lo, x).
Axes of the slice: x: 4, y: 4 (y_hi: 2, y_lo: 2; y = y_hi * 2 + y_lo), z: 8, core: 2. Of those that a mesh axis runs over, the one named last changes fastest.
Arguments:
- noisy: float32 [32, 512, 4096], P(None, 'gx', 'gy'), may hold values from -6 to 6
- weight: float32 [32, 512, 4096], P(None, 'gx', 'gy'), may hold values from 0.05 to 1
Outputs:
- denoised: float32 [32, 512, 4096], P(None, 'gx', 'gy')
The draws below stay inside these ranges and needn't reach their ends.
All inputs are finite; a program needn't handle non-finite values.
Results may differ from the reference program's by a relative error of at most 0.00002.
Values sent between devices are 32-bit elements; how exact they have to be, the bound alone decides.
No kernel may reach another device: no remote copies, remote signals or barrier semaphores. Data moves between devices by JAX's collectives and lax.ppermute only.
A program may use at most 192 MiB of HBM per device.

```python
import math
import jax
import jax.numpy as jnp
from jax import lax

PLANES = 32
ITERS = 8
NX = 512
NY = 4096


def shard_levels(rng, extent, pieces, least, high):
    level, own = 1.0, jax.random.fold_in(rng, 6)
    for dim, shards_of in pieces:
        draws = jnp.exp(jax.random.uniform(jax.random.fold_in(own, dim), (shards_of,), jnp.float32, least / len(pieces), high / len(pieces)))
        level = level * jnp.repeat(draws, extent[dim] // shards_of).reshape([-1 if axis == dim else 1 for axis in range(len(extent))])
    return level


def noise(own_key, extent, scale, limit, split=(), dtype=jnp.bfloat16):
    entries = scale * jax.random.normal(own_key, extent, jnp.float32)
    if split:
        entries = entries * shard_levels(own_key, extent, split, -0.22, 0.18)
    return jnp.clip(entries, -limit, limit).astype(dtype)


def setup_inputs(seed: int = 0) -> dict:
    splits = jax.random.split(jax.random.key(seed), 3)
    return {
        "noisy": noise(splits[0], (PLANES, NX, NY), 1.0, 6.0, ((1, 32), (2, 8)), jnp.float32),
        "weight": jnp.clip(jnp.exp(math.log(1.0) - 2.9957323 * jax.random.uniform(splits[1], (PLANES, NX, NY), jnp.float32) ** shard_levels(splits[1], (PLANES, NX, NY), ((1, 32), (2, 8)), -0.2, 0.2)), 0.05, 1.0),
    }


dual_step = 0.28
primal_step = 0.28
fidelity = 1.0

def forward(field, axis):
    count = field.shape[axis]
    diffs = lax.slice_in_dim(field, 1, count, axis=axis) - lax.slice_in_dim(field, 0, count - 1, axis=axis)
    edge = jnp.zeros_like(lax.slice_in_dim(field, 0, 1, axis=axis))
    return jnp.concatenate([diffs, edge], axis)

def backward(dual, axis):
    count = dual.shape[axis]
    edge = jnp.zeros_like(lax.slice_in_dim(dual, 0, 1, axis=axis))
    earlier = jnp.concatenate([edge, lax.slice_in_dim(dual, 0, count - 1, axis=axis)], axis)
    return dual - earlier

def project(dual_x, dual_y, dual_z, weight):
    length = jnp.sqrt(dual_x * dual_x + dual_y * dual_y + dual_z * dual_z)
    factor = jnp.maximum(1.0, length / weight)
    return (dual_x / factor, dual_y / factor, dual_z / factor)

def reference(noisy, weight):
    primal = noisy
    extrapolated = noisy
    dual_x = jnp.zeros_like(noisy)
    dual_y = jnp.zeros_like(noisy)
    dual_z = jnp.zeros_like(noisy)
    for iteration in range(ITERS):
        dual_x = dual_x + dual_step * forward(extrapolated, 1)
        dual_y = dual_y + dual_step * forward(extrapolated, 2)
        dual_z = dual_z + dual_step * forward(extrapolated, 0)
        dual_x, dual_y, dual_z = project(dual_x, dual_y, dual_z, weight)
        divergence = backward(dual_x, 1) + backward(dual_y, 2) + backward(dual_z, 0)
        updated = (primal + primal_step * divergence + primal_step * fidelity * noisy) / (1.0 + primal_step * fidelity)
        extrapolated = 2.0 * updated - primal
        primal = updated
    return primal
```

```python
import jax
import jax.numpy as jnp
from jax import lax
from jax.sharding import PartitionSpec as P

ITERS = 8
HALO = ITERS


dual_step = 0.28
primal_step = 0.28
fidelity = 1.0


def from_offset(value, axis, offset):
    count = lax.axis_size(axis)
    return lax.ppermute(value, axis, [((dest + offset) % count, dest) for dest in range(count)])


def extend(noisy, weight):
    planes, rows, cols = noisy.shape
    width = -(-(cols + 2 * HALO) // 128) * 128
    both = jnp.stack([noisy, weight])
    right = from_offset(both[..., :HALO], "gy", 1)
    left = from_offset(both[..., cols - HALO:], "gy", -1)
    gap = width - cols - 2 * HALO
    filler = jnp.concatenate(
        [jnp.zeros((1, planes, rows, gap), noisy.dtype), jnp.ones((1, planes, rows, gap), noisy.dtype)], 0
    )
    wide = jnp.concatenate([both, right, filler, left], 3)
    below = from_offset(wide[:, :, :HALO, :], "gx", 1)
    above = from_offset(wide[:, :, rows - HALO:, :], "gx", -1)
    full = jnp.concatenate([wide, below, above], 2)
    return full[0], full[1], width


def along_z(field):
    edge = jnp.zeros_like(field[:1])
    return jnp.concatenate([field[1:] - field[:-1], edge], 0)


def back_z(dual):
    edge = jnp.zeros_like(dual[:1])
    return dual - jnp.concatenate([edge, dual[:-1]], 0)


def project(dual_x, dual_y, dual_z, weight):
    length = jnp.sqrt(dual_x * dual_x + dual_y * dual_y + dual_z * dual_z)
    factor = jnp.maximum(1.0, length / weight)
    return (dual_x / factor, dual_y / factor, dual_z / factor)


def per_device(noisy, weight):
    planes, rows_x, rows_y = noisy.shape
    total_x = rows_x * lax.axis_size("gx")
    total_y = rows_y * lax.axis_size("gy")
    start_x = lax.axis_index("gx") * rows_x
    start_y = lax.axis_index("gy") * rows_y
    noisy_e, weight_e, width = extend(noisy, weight)
    ext_x = rows_x + 2 * HALO

    local_x = jnp.arange(ext_x, dtype=jnp.int32)
    index_x = jnp.where(local_x >= rows_x + HALO, start_x + local_x - ext_x, start_x + local_x)
    keep_x = ((index_x >= 0) & (index_x < total_x - 1))[None, :, None]
    local_y = jnp.arange(width, dtype=jnp.int32)
    index_y = jnp.where(local_y >= width - HALO, start_y + local_y - width, start_y + local_y)
    inside_y = (local_y < rows_y + HALO) | (local_y >= width - HALO)
    keep_y = (inside_y & (index_y >= 0) & (index_y < total_y - 1))[None, None, :]

    primal = noisy_e
    extrapolated = noisy_e
    dual_x = jnp.zeros_like(noisy_e)
    dual_y = jnp.zeros_like(noisy_e)
    dual_z = jnp.zeros_like(noisy_e)
    for iteration in range(ITERS):
        slope_x = jnp.where(keep_x, jnp.roll(extrapolated, -1, 1) - extrapolated, 0.0)
        slope_y = jnp.where(keep_y, jnp.roll(extrapolated, -1, 2) - extrapolated, 0.0)
        dual_x = dual_x + dual_step * slope_x
        dual_y = dual_y + dual_step * slope_y
        dual_z = dual_z + dual_step * along_z(extrapolated)
        dual_x, dual_y, dual_z = project(dual_x, dual_y, dual_z, weight_e)
        diverge_x = dual_x - jnp.roll(dual_x, 1, 1)
        diverge_y = dual_y - jnp.roll(dual_y, 1, 2)
        divergence = diverge_x + diverge_y + back_z(dual_z)
        updated = (primal + primal_step * divergence + primal_step * fidelity * noisy_e) / (
            1.0 + primal_step * fidelity
        )
        extrapolated = 2.0 * updated - primal
        primal = updated
    return primal[:, :rows_x, :rows_y]


def solution(mesh):
    placed = (P(None, "gx", "gy"), P(None, "gx", "gy"))
    return jax.shard_map(
        per_device, mesh=mesh, in_specs=placed, out_specs=P(None, "gx", "gy"), check_vma=False
    )
```

```python
import functools

import jax
import jax.numpy as jnp
from jax import lax
from jax.experimental import pallas as pl
from jax.experimental.pallas import tpu as pltpu
from jax.sharding import PartitionSpec as P

ITERS = 8
HALO = ITERS


dual_step = 0.28
primal_step = 0.28
fidelity = 1.0


def from_offset(value, axis, offset):
    count = lax.axis_size(axis)
    return lax.ppermute(value, axis, [((dest + offset) % count, dest) for dest in range(count)])


def extend(noisy, weight):
    planes, rows, cols = noisy.shape
    width = -(-(cols + 2 * HALO) // 128) * 128
    both = jnp.stack([noisy, weight])
    right = from_offset(both[..., :HALO], "gy", 1)
    left = from_offset(both[..., cols - HALO:], "gy", -1)
    gap = width - cols - 2 * HALO
    filler = jnp.concatenate(
        [jnp.zeros((1, planes, rows, gap), noisy.dtype), jnp.ones((1, planes, rows, gap), noisy.dtype)], 0
    )
    wide = jnp.concatenate([both, right, filler, left], 3)
    below = from_offset(wide[:, :, :HALO, :], "gx", 1)
    above = from_offset(wide[:, :, rows - HALO:, :], "gx", -1)
    full = jnp.concatenate([wide, below, above], 2)
    return full[0], full[1], width


def iterate_kernel(noisy_ref, weight_ref, keep_x_ref, keep_y_ref, out_ref, primal, extrapolated, dual_x, dual_y, dual_z):
    planes, rows, width = noisy_ref.shape
    primal[...] = noisy_ref[...]
    extrapolated[...] = noisy_ref[...]
    dual_x[...] = jnp.zeros_like(noisy_ref)
    dual_y[...] = jnp.zeros_like(noisy_ref)
    dual_z[...] = jnp.zeros_like(noisy_ref)
    keep_x = keep_x_ref[...] > 0.5
    keep_y = keep_y_ref[...] > 0.5

    def plane(z, dual_z_before):
        here = extrapolated[z]
        after = extrapolated[jnp.minimum(z + 1, planes - 1)]
        slope_x = jnp.where(keep_x, pltpu.roll(here, rows - 1, 0) - here, 0.0)
        slope_y = jnp.where(keep_y, pltpu.roll(here, width - 1, 1) - here, 0.0)
        slope_z = jnp.where(z < planes - 1, after - here, 0.0)
        new_x, new_y, new_z = project(
            dual_x[z] + dual_step * slope_x,
            dual_y[z] + dual_step * slope_y,
            dual_z[z] + dual_step * slope_z,
            weight_ref[z],
        )
        dual_x[z] = new_x
        dual_y[z] = new_y
        dual_z[z] = new_z
        divergence = (
            (new_x - pltpu.roll(new_x, 1, 0)) + (new_y - pltpu.roll(new_y, 1, 1)) + (new_z - dual_z_before)
        )
        old = primal[z]
        updated = (old + primal_step * divergence + primal_step * fidelity * noisy_ref[z]) / (
            1.0 + primal_step * fidelity
        )
        extrapolated[z] = 2.0 * updated - old
        primal[z] = updated
        return new_z

    for iteration in range(ITERS):
        lax.fori_loop(0, planes, plane, jnp.zeros((rows, width), jnp.float32))
    own_rows, own_cols = out_ref.shape[1:]
    out_ref[...] = primal[:, :own_rows, :own_cols]


def project(dual_x, dual_y, dual_z, weight):
    length = jnp.sqrt(dual_x * dual_x + dual_y * dual_y + dual_z * dual_z)
    factor = jnp.maximum(1.0, length / weight)
    return (dual_x / factor, dual_y / factor, dual_z / factor)


def per_device(noisy, weight):
    planes, rows_x, rows_y = noisy.shape
    total_x = rows_x * lax.axis_size("gx")
    total_y = rows_y * lax.axis_size("gy")
    start_x = lax.axis_index("gx") * rows_x
    start_y = lax.axis_index("gy") * rows_y
    noisy_e, weight_e, width = extend(noisy, weight)
    ext_x = rows_x + 2 * HALO

    local_x = jnp.arange(ext_x, dtype=jnp.int32)
    index_x = jnp.where(local_x >= rows_x + HALO, start_x + local_x - ext_x, start_x + local_x)
    keep_x = (index_x >= 0) & (index_x < total_x - 1)
    local_y = jnp.arange(width, dtype=jnp.int32)
    index_y = jnp.where(local_y >= width - HALO, start_y + local_y - width, start_y + local_y)
    inside_y = (local_y < rows_y + HALO) | (local_y >= width - HALO)
    keep_y = inside_y & (index_y >= 0) & (index_y < total_y - 1)
    keep_x = jnp.broadcast_to(keep_x[:, None], (ext_x, width)).astype(jnp.float32)
    keep_y = jnp.broadcast_to(keep_y[None, :], (ext_x, width)).astype(jnp.float32)

    field = jax.ShapeDtypeStruct((planes, ext_x, width), jnp.float32)
    vmem = pl.BlockSpec(memory_space=pltpu.VMEM)
    return pl.pallas_call(
        iterate_kernel,
        out_shape=jax.ShapeDtypeStruct(noisy.shape, jnp.float32),
        in_specs=[vmem] * 4,
        out_specs=vmem,
        scratch_shapes=[pltpu.VMEM(field.shape, jnp.float32)] * 5,
        compiler_params=pltpu.CompilerParams(vmem_limit_bytes=48 * 1024 * 1024),
    )(noisy_e, weight_e, keep_x, keep_y)


def solution(mesh):
    placed = (P(None, "gx", "gy"), P(None, "gx", "gy"))
    return jax.shard_map(
        per_device, mesh=mesh, in_specs=placed, out_specs=P(None, "gx", "gy"), check_vma=False
    )
```

```python
import functools

import jax
import jax.numpy as jnp
from jax import lax
from jax.experimental import pallas as pl
from jax.experimental.pallas import tpu as pltpu
from jax.sharding import PartitionSpec as P

ITERS = 8
HALO = ITERS


dual_step = 0.28
primal_step = 0.28
fidelity = 1.0


def from_offset(value, axis, offset):
    count = lax.axis_size(axis)
    return lax.ppermute(value, axis, [((dest + offset) % count, dest) for dest in range(count)])


def extend(noisy, weight):
    planes, rows, cols = noisy.shape
    width = -(-(cols + 2 * HALO) // 128) * 128
    both = jnp.stack([noisy, weight])
    right = from_offset(both[..., :HALO], "gy", 1)
    left = from_offset(both[..., cols - HALO:], "gy", -1)
    gap = width - cols - 2 * HALO
    filler = jnp.concatenate(
        [jnp.zeros((1, planes, rows, gap), noisy.dtype), jnp.ones((1, planes, rows, gap), noisy.dtype)], 0
    )
    wide = jnp.concatenate([both, right, filler, left], 3)
    below = from_offset(wide[:, :, :HALO, :], "gx", 1)
    above = from_offset(wide[:, :, rows - HALO:, :], "gx", -1)
    full = jnp.concatenate([wide, below, above], 2)
    return full[0], full[1], width


def iterate_kernel(
    noisy_ref, weight_ref, keep_x_ref, keep_y_ref, out_ref, primal, extrapolated, dual_x, dual_y, dual_z, inverse_weight
):
    planes, rows, width = noisy_ref.shape
    primal[...] = noisy_ref[...]
    extrapolated[...] = noisy_ref[...]
    dual_x[...] = jnp.zeros_like(noisy_ref)
    dual_y[...] = jnp.zeros_like(noisy_ref)
    dual_z[...] = jnp.zeros_like(noisy_ref)
    keep_x = keep_x_ref[...] > 0.5
    keep_y = keep_y_ref[...] > 0.5
    inverse_weight[...] = 1.0 / weight_ref[...]
    shrink = 1.0 / (1.0 + primal_step * fidelity)

    def plane(z, dual_z_before):
        here = extrapolated[z]
        after = extrapolated[jnp.minimum(z + 1, planes - 1)]
        slope_x = jnp.where(keep_x, pltpu.roll(here, rows - 1, 0) - here, 0.0)
        slope_y = jnp.where(keep_y, pltpu.roll(here, width - 1, 1) - here, 0.0)
        slope_z = jnp.where(z < planes - 1, after - here, 0.0)
        new_x, new_y, new_z = project(
            dual_x[z] + dual_step * slope_x,
            dual_y[z] + dual_step * slope_y,
            dual_z[z] + dual_step * slope_z,
            inverse_weight[z],
        )
        dual_x[z] = new_x
        dual_y[z] = new_y
        dual_z[z] = new_z
        divergence = (
            (new_x - pltpu.roll(new_x, 1, 0)) + (new_y - pltpu.roll(new_y, 1, 1)) + (new_z - dual_z_before)
        )
        old = primal[z]
        updated = (old + primal_step * divergence + primal_step * fidelity * noisy_ref[z]) * shrink
        extrapolated[z] = 2.0 * updated - old
        primal[z] = updated
        return new_z

    for iteration in range(ITERS):
        lax.fori_loop(0, planes, plane, jnp.zeros((rows, width), jnp.float32))
    own_rows, own_cols = out_ref.shape[1:]
    out_ref[...] = primal[:, :own_rows, :own_cols]


def project(dual_x, dual_y, dual_z, inverse_weight):
    length = jnp.sqrt(dual_x * dual_x + dual_y * dual_y + dual_z * dual_z)
    scale = 1.0 / jnp.maximum(1.0, length * inverse_weight)
    return (dual_x * scale, dual_y * scale, dual_z * scale)


def per_device(noisy, weight):
    planes, rows_x, rows_y = noisy.shape
    total_x = rows_x * lax.axis_size("gx")
    total_y = rows_y * lax.axis_size("gy")
    start_x = lax.axis_index("gx") * rows_x
    start_y = lax.axis_index("gy") * rows_y
    noisy_e, weight_e, width = extend(noisy, weight)
    ext_x = rows_x + 2 * HALO

    local_x = jnp.arange(ext_x, dtype=jnp.int32)
    index_x = jnp.where(local_x >= rows_x + HALO, start_x + local_x - ext_x, start_x + local_x)
    keep_x = (index_x >= 0) & (index_x < total_x - 1)
    local_y = jnp.arange(width, dtype=jnp.int32)
    index_y = jnp.where(local_y >= width - HALO, start_y + local_y - width, start_y + local_y)
    inside_y = (local_y < rows_y + HALO) | (local_y >= width - HALO)
    keep_y = inside_y & (index_y >= 0) & (index_y < total_y - 1)
    keep_x = jnp.broadcast_to(keep_x[:, None], (ext_x, width)).astype(jnp.float32)
    keep_y = jnp.broadcast_to(keep_y[None, :], (ext_x, width)).astype(jnp.float32)

    field = jax.ShapeDtypeStruct((planes, ext_x, width), jnp.float32)
    vmem = pl.BlockSpec(memory_space=pltpu.VMEM)
    return pl.pallas_call(
        iterate_kernel,
        out_shape=jax.ShapeDtypeStruct(noisy.shape, jnp.float32),
        in_specs=[vmem] * 4,
        out_specs=vmem,
        scratch_shapes=[pltpu.VMEM(field.shape, jnp.float32)] * 6,
        compiler_params=pltpu.CompilerParams(vmem_limit_bytes=48 * 1024 * 1024),
    )(noisy_e, weight_e, keep_x, keep_y)


def solution(mesh):
    placed = (P(None, "gx", "gy"), P(None, "gx", "gy"))
    return jax.shard_map(
        per_device, mesh=mesh, in_specs=placed, out_specs=P(None, "gx", "gy"), check_vma=False
    )
```

```python
import functools

import jax
import jax.numpy as jnp
from jax import lax
from jax.experimental import pallas as pl
from jax.experimental.pallas import tpu as pltpu
from jax.sharding import PartitionSpec as P

ITERS = 8
HALO = ITERS


dual_step = 0.28
primal_step = 0.28
fidelity = 1.0


def from_offset(value, step_x, step_y):
    count_x, count_y = lax.axis_size("gx"), lax.axis_size("gy")
    pairs = []
    for dest_x in range(count_x):
        for dest_y in range(count_y):
            source = ((dest_x + step_x) % count_x) * count_y + (dest_y + step_y) % count_y
            pairs.append((source, dest_x * count_y + dest_y))
    axes = tuple(name for name, step in (("gx", step_x), ("gy", step_y)) if step)
    if len(axes) == 1:
        pairs = [(source % count_y, dest % count_y) if axes == ("gy",) else (source // count_y, dest // count_y)
                 for source, dest in pairs]
        pairs = sorted(set(pairs))
        return lax.ppermute(value, axes[0], pairs)
    return lax.ppermute(value, axes, pairs)


def extend(noisy, weight):
    planes, rows, cols = noisy.shape
    width = -(-(cols + 2 * HALO) // 128) * 128
    both = jnp.stack([noisy, weight])
    first_rows, last_rows = both[:, :, :HALO, :], both[:, :, rows - HALO:, :]
    below = from_offset(first_rows, 1, 0)
    above = from_offset(last_rows, -1, 0)
    right = from_offset(both[..., :HALO], 0, 1)
    left = from_offset(both[..., cols - HALO:], 0, -1)
    below_right = from_offset(first_rows[..., :HALO], 1, 1)
    below_left = from_offset(first_rows[..., cols - HALO:], 1, -1)
    above_right = from_offset(last_rows[..., :HALO], -1, 1)
    above_left = from_offset(last_rows[..., cols - HALO:], -1, -1)
    gap = width - cols - 2 * HALO

    def band(middle, after, before):
        count = middle.shape[2]
        filler = jnp.concatenate(
            [jnp.zeros((1, planes, count, gap), noisy.dtype), jnp.ones((1, planes, count, gap), noisy.dtype)], 0
        )
        return jnp.concatenate([middle, after, filler, before], 3)

    full = jnp.concatenate(
        [band(both, right, left), band(below, below_right, below_left), band(above, above_right, above_left)], 2
    )
    return full[0], full[1], width


def iterate_kernel(
    noisy_ref, weight_ref, keep_x_ref, keep_y_ref, out_ref, primal, extrapolated, dual_x, dual_y, dual_z, inverse_weight
):
    planes, rows, width = noisy_ref.shape
    primal[...] = noisy_ref[...]
    extrapolated[...] = noisy_ref[...]
    dual_x[...] = jnp.zeros_like(noisy_ref)
    dual_y[...] = jnp.zeros_like(noisy_ref)
    dual_z[...] = jnp.zeros_like(noisy_ref)
    keep_x = keep_x_ref[...] > 0.5
    keep_y = keep_y_ref[...] > 0.5
    inverse_weight[...] = 1.0 / weight_ref[...]
    shrink = 1.0 / (1.0 + primal_step * fidelity)

    def plane(z, dual_z_before):
        here = extrapolated[z]
        after = extrapolated[jnp.minimum(z + 1, planes - 1)]
        slope_x = jnp.where(keep_x, pltpu.roll(here, rows - 1, 0) - here, 0.0)
        slope_y = jnp.where(keep_y, pltpu.roll(here, width - 1, 1) - here, 0.0)
        slope_z = jnp.where(z < planes - 1, after - here, 0.0)
        new_x, new_y, new_z = project(
            dual_x[z] + dual_step * slope_x,
            dual_y[z] + dual_step * slope_y,
            dual_z[z] + dual_step * slope_z,
            inverse_weight[z],
        )
        dual_x[z] = new_x
        dual_y[z] = new_y
        dual_z[z] = new_z
        divergence = (
            (new_x - pltpu.roll(new_x, 1, 0)) + (new_y - pltpu.roll(new_y, 1, 1)) + (new_z - dual_z_before)
        )
        old = primal[z]
        updated = (old + primal_step * divergence + primal_step * fidelity * noisy_ref[z]) * shrink
        extrapolated[z] = 2.0 * updated - old
        primal[z] = updated
        return new_z

    for iteration in range(ITERS):
        lax.fori_loop(0, planes, plane, jnp.zeros((rows, width), jnp.float32))
    own_rows, own_cols = out_ref.shape[1:]
    out_ref[...] = primal[:, :own_rows, :own_cols]


def project(dual_x, dual_y, dual_z, inverse_weight):
    length = jnp.sqrt(dual_x * dual_x + dual_y * dual_y + dual_z * dual_z)
    scale = 1.0 / jnp.maximum(1.0, length * inverse_weight)
    return (dual_x * scale, dual_y * scale, dual_z * scale)


def per_device(noisy, weight):
    planes, rows_x, rows_y = noisy.shape
    total_x = rows_x * lax.axis_size("gx")
    total_y = rows_y * lax.axis_size("gy")
    start_x = lax.axis_index("gx") * rows_x
    start_y = lax.axis_index("gy") * rows_y
    noisy_e, weight_e, width = extend(noisy, weight)
    ext_x = rows_x + 2 * HALO

    local_x = jnp.arange(ext_x, dtype=jnp.int32)
    index_x = jnp.where(local_x >= rows_x + HALO, start_x + local_x - ext_x, start_x + local_x)
    keep_x = (index_x >= 0) & (index_x < total_x - 1)
    local_y = jnp.arange(width, dtype=jnp.int32)
    index_y = jnp.where(local_y >= width - HALO, start_y + local_y - width, start_y + local_y)
    inside_y = (local_y < rows_y + HALO) | (local_y >= width - HALO)
    keep_y = inside_y & (index_y >= 0) & (index_y < total_y - 1)
    keep_x = jnp.broadcast_to(keep_x[:, None], (ext_x, width)).astype(jnp.float32)
    keep_y = jnp.broadcast_to(keep_y[None, :], (ext_x, width)).astype(jnp.float32)

    field = jax.ShapeDtypeStruct((planes, ext_x, width), jnp.float32)
    vmem = pl.BlockSpec(memory_space=pltpu.VMEM)
    return pl.pallas_call(
        iterate_kernel,
        out_shape=jax.ShapeDtypeStruct(noisy.shape, jnp.float32),
        in_specs=[vmem] * 4,
        out_specs=vmem,
        scratch_shapes=[pltpu.VMEM(field.shape, jnp.float32)] * 6,
        compiler_params=pltpu.CompilerParams(vmem_limit_bytes=48 * 1024 * 1024),
    )(noisy_e, weight_e, keep_x, keep_y)


def solution(mesh):
    placed = (P(None, "gx", "gy"), P(None, "gx", "gy"))
    return jax.shard_map(
        per_device, mesh=mesh, in_specs=placed, out_specs=P(None, "gx", "gy"), check_vma=False
    )
```

```python
import functools

import jax
import jax.numpy as jnp
from jax import lax
from jax.experimental import pallas as pl
from jax.experimental.pallas import tpu as pltpu
from jax.sharding import PartitionSpec as P

ITERS = 8
HALO = ITERS


dual_step = 0.28
primal_step = 0.28
fidelity = 1.0


def from_offset(value, axis, offset):
    count = lax.axis_size(axis)
    return lax.ppermute(value, axis, [((dest + offset) % count, dest) for dest in range(count)])


def extend(noisy, weight):
    planes, rows, cols = noisy.shape
    width = -(-(cols + 2 * HALO) // 128) * 128
    both = jnp.stack([noisy, weight])
    right = from_offset(both[..., :HALO], "gy", 1)
    left = from_offset(both[..., cols - HALO:], "gy", -1)
    gap = width - cols - 2 * HALO
    filler = jnp.concatenate(
        [jnp.zeros((1, planes, rows, gap), noisy.dtype), jnp.ones((1, planes, rows, gap), noisy.dtype)], 0
    )
    wide = jnp.concatenate([both, right, filler, left], 3)
    below = from_offset(wide[:, :, :HALO, :], "gx", 1)
    above = from_offset(wide[:, :, rows - HALO:, :], "gx", -1)
    full = jnp.concatenate([wide, below, above], 2)
    return full[0], full[1], width


LANES = 128


def iterate_kernel(
    noisy_ref, weight_ref, step_x_ref, step_y_ref, out_ref,
    primal, extrapolated, dual_x, dual_y, dual_z, pulled,
):
    planes, rows, width = noisy_ref.shape
    blocks = width // LANES
    shrink = 1.0 / (1.0 + primal_step * fidelity)

    def setup(z, carry):
        noisy = noisy_ref[z]
        primal[z] = noisy
        extrapolated[z] = noisy
        pulled[z] = primal_step * fidelity * noisy
        dual_x[z] = jnp.zeros_like(noisy)
        dual_y[z] = jnp.zeros_like(noisy)
        dual_z[z] = jnp.zeros_like(noisy)
        return carry

    lax.fori_loop(0, planes, setup, 0)
    lane = lax.broadcasted_iota(jnp.int32, (rows, LANES), 1)
    last_lane = lane == LANES - 1
    first_lane = lane == 0

    def plane(z, carry):
        after = jnp.minimum(z + 1, planes - 1)
        before = jnp.maximum(z - 1, 0)
        step_z = jnp.where(z < planes - 1, dual_step, 0.0)
        turned = [pltpu.roll(extrapolated[z, :, pl.ds(block * LANES, LANES)], LANES - 1, 1) for block in range(blocks)]
        for block in range(blocks):
            cols = pl.ds(block * LANES, LANES)
            here = extrapolated[z, :, cols]
            next_y = jnp.where(last_lane, turned[(block + 1) % blocks], turned[block])
            next_x = pltpu.roll(here, rows - 1, 0)
            new_x, new_y, new_z = project(
                dual_x[z, :, cols] + step_x_ref[:, cols] * (next_x - here),
                dual_y[z, :, cols] + step_y_ref[:, cols] * (next_y - here),
                dual_z[z, :, cols] + step_z * (extrapolated[after, :, cols] - here),
                weight_ref[z, :, cols],
            )
            dual_x[z, :, cols] = new_x
            dual_y[z, :, cols] = new_y
            dual_z[z, :, cols] = new_z
        turned = [pltpu.roll(dual_y[z, :, pl.ds(block * LANES, LANES)], 1, 1) for block in range(blocks)]
        for block in range(blocks):
            cols = pl.ds(block * LANES, LANES)
            new_x = dual_x[z, :, cols]
            new_y = dual_y[z, :, cols]
            prev_y = jnp.where(first_lane, turned[(block - 1) % blocks], turned[block])
            prev_z = jnp.where(z > 0, dual_z[before, :, cols], 0.0)
            divergence = (new_x - pltpu.roll(new_x, 1, 0)) + (new_y - prev_y) + (dual_z[z, :, cols] - prev_z)
            old = primal[z, :, cols]
            updated = (old + primal_step * divergence + pulled[z, :, cols]) * shrink
            extrapolated[z, :, cols] = 2.0 * updated - old
            primal[z, :, cols] = updated
        return carry

    for iteration in range(ITERS):
        lax.fori_loop(0, planes, plane, 0)
    own_rows, own_cols = out_ref.shape[1:]
    out_ref[...] = primal[:, :own_rows, :own_cols]


def project(dual_x, dual_y, dual_z, weight):
    scale = jnp.minimum(1.0, weight * lax.rsqrt(dual_x * dual_x + dual_y * dual_y + dual_z * dual_z))
    return (dual_x * scale, dual_y * scale, dual_z * scale)


def per_device(noisy, weight):
    planes, rows_x, rows_y = noisy.shape
    total_x = rows_x * lax.axis_size("gx")
    total_y = rows_y * lax.axis_size("gy")
    start_x = lax.axis_index("gx") * rows_x
    start_y = lax.axis_index("gy") * rows_y
    noisy_e, weight_e, width = extend(noisy, weight)
    ext_x = rows_x + 2 * HALO

    local_x = jnp.arange(ext_x, dtype=jnp.int32)
    index_x = jnp.where(local_x >= rows_x + HALO, start_x + local_x - ext_x, start_x + local_x)
    keep_x = (index_x >= 0) & (index_x < total_x - 1)
    local_y = jnp.arange(width, dtype=jnp.int32)
    index_y = jnp.where(local_y >= width - HALO, start_y + local_y - width, start_y + local_y)
    inside_y = (local_y < rows_y + HALO) | (local_y >= width - HALO)
    keep_y = inside_y & (index_y >= 0) & (index_y < total_y - 1)
    step_x = jnp.broadcast_to(jnp.where(keep_x, dual_step, 0.0)[:, None], (ext_x, width)).astype(jnp.float32)
    step_y = jnp.broadcast_to(jnp.where(keep_y, dual_step, 0.0)[None, :], (ext_x, width)).astype(jnp.float32)

    field = jax.ShapeDtypeStruct((planes, ext_x, width), jnp.float32)
    vmem = pl.BlockSpec(memory_space=pltpu.VMEM)
    return pl.pallas_call(
        iterate_kernel,
        out_shape=jax.ShapeDtypeStruct(noisy.shape, jnp.float32),
        in_specs=[vmem] * 4,
        out_specs=vmem,
        scratch_shapes=[pltpu.VMEM(field.shape, jnp.float32)] * 6,
        compiler_params=pltpu.CompilerParams(vmem_limit_bytes=48 * 1024 * 1024),
    )(noisy_e, weight_e, step_x, step_y)


def solution(mesh):
    placed = (P(None, "gx", "gy"), P(None, "gx", "gy"))
    return jax.shard_map(
        per_device, mesh=mesh, in_specs=placed, out_specs=P(None, "gx", "gy"), check_vma=False
    )
```

```python
import functools

import jax
import jax.numpy as jnp
from jax import lax
from jax.experimental import pallas as pl
from jax.experimental.pallas import tpu as pltpu
from jax.sharding import PartitionSpec as P

ITERS = 8
HALO = ITERS


dual_step = 0.28
primal_step = 0.28
fidelity = 1.0


def from_offset(value, axis, offset):
    count = lax.axis_size(axis)
    return lax.ppermute(value, axis, [((dest + offset) % count, dest) for dest in range(count)])


def extend(noisy, weight):
    planes, rows, cols = noisy.shape
    width = -(-(cols + 2 * HALO) // 128) * 128
    both = jnp.stack([noisy, weight])
    right = from_offset(both[..., :HALO], "gy", 1)
    left = from_offset(both[..., cols - HALO:], "gy", -1)
    gap = width - cols - 2 * HALO
    filler = jnp.concatenate(
        [jnp.zeros((1, planes, rows, gap), noisy.dtype), jnp.ones((1, planes, rows, gap), noisy.dtype)], 0
    )
    tail = jnp.concatenate([right, filler, left], 3)
    first = jnp.concatenate([both[:, :, :HALO, :], tail[:, :, :HALO, :]], 3)
    last = jnp.concatenate([both[:, :, rows - HALO:, :], tail[:, :, rows - HALO:, :]], 3)
    below = from_offset(first, "gx", 1)
    above = from_offset(last, "gx", -1)
    return tail, below, above, width


LANES = 128


def iterate_kernel(
    own_noisy_ref, own_weight_ref, tail_ref, below_ref, above_ref, step_x_ref, step_y_ref, out_ref,
    noisy_ref, weight_ref, primal, extrapolated, dual_x, dual_y, dual_z, pulled,
):
    planes, rows, width = noisy_ref.shape
    own_rows, own_cols = out_ref.shape[1:]
    halo = below_ref.shape[2]
    blocks = width // LANES
    shrink = 1.0 / (1.0 + primal_step * fidelity)

    def setup(z, carry):
        for field, own_ref, part in ((noisy_ref, own_noisy_ref, 0), (weight_ref, own_weight_ref, 1)):
            field[z, pl.ds(0, own_rows), pl.ds(0, own_cols)] = own_ref[z]
            field[z, pl.ds(0, own_rows), pl.ds(own_cols, width - own_cols)] = tail_ref[part, z]
            field[z, pl.ds(own_rows, halo)] = below_ref[part, z]
            field[z, pl.ds(own_rows + halo, halo)] = above_ref[part, z]
        noisy = noisy_ref[z]
        primal[z] = noisy
        extrapolated[z] = noisy
        pulled[z] = primal_step * fidelity * noisy
        dual_x[z] = jnp.zeros_like(noisy)
        dual_y[z] = jnp.zeros_like(noisy)
        dual_z[z] = jnp.zeros_like(noisy)
        return carry

    lax.fori_loop(0, planes, setup, 0)
    lane = lax.broadcasted_iota(jnp.int32, (rows, LANES), 1)
    last_lane = lane == LANES - 1
    first_lane = lane == 0

    def plane(z, carry):
        after = jnp.minimum(z + 1, planes - 1)
        before = jnp.maximum(z - 1, 0)
        step_z = jnp.where(z < planes - 1, dual_step, 0.0)
        turned = [pltpu.roll(extrapolated[z, :, pl.ds(block * LANES, LANES)], LANES - 1, 1) for block in range(blocks)]
        for block in range(blocks):
            cols = pl.ds(block * LANES, LANES)
            here = extrapolated[z, :, cols]
            next_y = jnp.where(last_lane, turned[(block + 1) % blocks], turned[block])
            next_x = pltpu.roll(here, rows - 1, 0)
            new_x, new_y, new_z = project(
                dual_x[z, :, cols] + step_x_ref[:, cols] * (next_x - here),
                dual_y[z, :, cols] + step_y_ref[:, cols] * (next_y - here),
                dual_z[z, :, cols] + step_z * (extrapolated[after, :, cols] - here),
                weight_ref[z, :, cols],
            )
            dual_x[z, :, cols] = new_x
            dual_y[z, :, cols] = new_y
            dual_z[z, :, cols] = new_z
        turned = [pltpu.roll(dual_y[z, :, pl.ds(block * LANES, LANES)], 1, 1) for block in range(blocks)]
        for block in range(blocks):
            cols = pl.ds(block * LANES, LANES)
            new_x = dual_x[z, :, cols]
            new_y = dual_y[z, :, cols]
            prev_y = jnp.where(first_lane, turned[(block - 1) % blocks], turned[block])
            prev_z = jnp.where(z > 0, dual_z[before, :, cols], 0.0)
            divergence = (new_x - pltpu.roll(new_x, 1, 0)) + (new_y - prev_y) + (dual_z[z, :, cols] - prev_z)
            old = primal[z, :, cols]
            updated = (old + primal_step * divergence + pulled[z, :, cols]) * shrink
            extrapolated[z, :, cols] = 2.0 * updated - old
            primal[z, :, cols] = updated
        return carry

    for iteration in range(ITERS):
        lax.fori_loop(0, planes, plane, 0)
    out_ref[...] = primal[:, :own_rows, :own_cols]


def project(dual_x, dual_y, dual_z, weight):
    scale = jnp.minimum(1.0, weight * lax.rsqrt(dual_x * dual_x + dual_y * dual_y + dual_z * dual_z))
    return (dual_x * scale, dual_y * scale, dual_z * scale)


def per_device(noisy, weight):
    planes, rows_x, rows_y = noisy.shape
    total_x = rows_x * lax.axis_size("gx")
    total_y = rows_y * lax.axis_size("gy")
    start_x = lax.axis_index("gx") * rows_x
    start_y = lax.axis_index("gy") * rows_y
    tail, below, above, width = extend(noisy, weight)
    ext_x = rows_x + 2 * HALO

    local_x = jnp.arange(ext_x, dtype=jnp.int32)
    index_x = jnp.where(local_x >= rows_x + HALO, start_x + local_x - ext_x, start_x + local_x)
    keep_x = (index_x >= 0) & (index_x < total_x - 1)
    local_y = jnp.arange(width, dtype=jnp.int32)
    index_y = jnp.where(local_y >= width - HALO, start_y + local_y - width, start_y + local_y)
    inside_y = (local_y < rows_y + HALO) | (local_y >= width - HALO)
    keep_y = inside_y & (index_y >= 0) & (index_y < total_y - 1)
    step_x = jnp.broadcast_to(jnp.where(keep_x, dual_step, 0.0)[:, None], (ext_x, width)).astype(jnp.float32)
    step_y = jnp.broadcast_to(jnp.where(keep_y, dual_step, 0.0)[None, :], (ext_x, width)).astype(jnp.float32)

    field = jax.ShapeDtypeStruct((planes, ext_x, width), jnp.float32)
    vmem = pl.BlockSpec(memory_space=pltpu.VMEM)
    return pl.pallas_call(
        iterate_kernel,
        out_shape=jax.ShapeDtypeStruct(noisy.shape, jnp.float32),
        in_specs=[vmem] * 7,
        out_specs=vmem,
        scratch_shapes=[pltpu.VMEM(field.shape, jnp.float32)] * 8,
        compiler_params=pltpu.CompilerParams(vmem_limit_bytes=48 * 1024 * 1024),
    )(noisy, weight, tail, below, above, step_x, step_y)


def solution(mesh):
    placed = (P(None, "gx", "gy"), P(None, "gx", "gy"))
    return jax.shard_map(
        per_device, mesh=mesh, in_specs=placed, out_specs=P(None, "gx", "gy"), check_vma=False
    )
```

```python
import functools

import jax
import jax.numpy as jnp
from jax import lax
from jax.experimental import pallas as pl
from jax.experimental.pallas import tpu as pltpu
from jax.sharding import PartitionSpec as P

ITERS = 8
HALO = ITERS


dual_step = 0.28
primal_step = 0.28
fidelity = 1.0


def from_offset(value, axis, offset):
    count = lax.axis_size(axis)
    return lax.ppermute(value, axis, [((dest + offset) % count, dest) for dest in range(count)])


def extend(noisy, weight):
    planes, rows, cols = noisy.shape
    width = -(-(cols + 2 * HALO) // 128) * 128
    both = jnp.stack([noisy, weight])
    right = from_offset(both[..., :HALO], "gy", 1)
    left = from_offset(both[..., cols - HALO:], "gy", -1)
    gap = width - cols - 2 * HALO
    filler = jnp.concatenate(
        [jnp.zeros((1, planes, rows, gap), noisy.dtype), jnp.ones((1, planes, rows, gap), noisy.dtype)], 0
    )
    tail = jnp.concatenate([right, filler, left], 3)
    sides = jnp.concatenate([right, left], 3)

    def pack(band):
        edge, corner = both[:, :, band, :], sides[:, :, band, :]
        return jnp.concatenate([edge.reshape(2, planes * HALO, cols), corner.reshape(2, -1, cols)], 1)

    def unpack(slab):
        edge = slab[:, : planes * HALO].reshape(2, planes, HALO, cols)
        corner = slab[:, planes * HALO :].reshape(2, planes, HALO, 2 * HALO)
        after, before = corner[..., :HALO], corner[..., HALO:]
        band_filler = filler[:, :, :HALO, :]
        return edge, jnp.concatenate([after, band_filler, before], 3)

    below = unpack(from_offset(pack(slice(0, HALO)), "gx", 1))
    above = unpack(from_offset(pack(slice(rows - HALO, rows)), "gx", -1))
    return tail, below, above, width


LANES = 128


def iterate_kernel(
    own_noisy_ref, own_weight_ref, tail_ref, below_ref, below_tail_ref, above_ref, above_tail_ref,
    step_x_ref, step_y_ref, out_ref,
    noisy_ref, weight_ref, primal, extrapolated, dual_x, dual_y, dual_z, pulled,
):
    planes, rows, width = noisy_ref.shape
    own_rows, own_cols = out_ref.shape[1:]
    halo = below_ref.shape[2]
    blocks = width // LANES
    shrink = 1.0 / (1.0 + primal_step * fidelity)

    def setup(z, carry):
        for field, own_ref, part in ((noisy_ref, own_noisy_ref, 0), (weight_ref, own_weight_ref, 1)):
            field[z, pl.ds(0, own_rows), pl.ds(0, own_cols)] = own_ref[z]
            field[z, pl.ds(0, own_rows), pl.ds(own_cols, width - own_cols)] = tail_ref[part, z]
            for offset, (edge_ref, corner_ref) in ((own_rows, (below_ref, below_tail_ref)),
                                                   (own_rows + halo, (above_ref, above_tail_ref))):
                field[z, pl.ds(offset, halo), pl.ds(0, own_cols)] = edge_ref[part, z]
                field[z, pl.ds(offset, halo), pl.ds(own_cols, width - own_cols)] = corner_ref[part, z]
        noisy = noisy_ref[z]
        primal[z] = noisy
        extrapolated[z] = noisy
        pulled[z] = primal_step * fidelity * noisy
        dual_x[z] = jnp.zeros_like(noisy)
        dual_y[z] = jnp.zeros_like(noisy)
        dual_z[z] = jnp.zeros_like(noisy)
        return carry

    lax.fori_loop(0, planes, setup, 0)
    lane = lax.broadcasted_iota(jnp.int32, (rows, LANES), 1)
    last_lane = lane == LANES - 1
    first_lane = lane == 0

    def plane(z, carry):
        after = jnp.minimum(z + 1, planes - 1)
        before = jnp.maximum(z - 1, 0)
        step_z = jnp.where(z < planes - 1, dual_step, 0.0)
        turned = [pltpu.roll(extrapolated[z, :, pl.ds(block * LANES, LANES)], LANES - 1, 1) for block in range(blocks)]
        for block in range(blocks):
            cols = pl.ds(block * LANES, LANES)
            here = extrapolated[z, :, cols]
            next_y = jnp.where(last_lane, turned[(block + 1) % blocks], turned[block])
            next_x = pltpu.roll(here, rows - 1, 0)
            new_x, new_y, new_z = project(
                dual_x[z, :, cols] + step_x_ref[:, cols] * (next_x - here),
                dual_y[z, :, cols] + step_y_ref[:, cols] * (next_y - here),
                dual_z[z, :, cols] + step_z * (extrapolated[after, :, cols] - here),
                weight_ref[z, :, cols],
            )
            dual_x[z, :, cols] = new_x
            dual_y[z, :, cols] = new_y
            dual_z[z, :, cols] = new_z
        turned = [pltpu.roll(dual_y[z, :, pl.ds(block * LANES, LANES)], 1, 1) for block in range(blocks)]
        for block in range(blocks):
            cols = pl.ds(block * LANES, LANES)
            new_x = dual_x[z, :, cols]
            new_y = dual_y[z, :, cols]
            prev_y = jnp.where(first_lane, turned[(block - 1) % blocks], turned[block])
            prev_z = jnp.where(z > 0, dual_z[before, :, cols], 0.0)
            divergence = (new_x - pltpu.roll(new_x, 1, 0)) + (new_y - prev_y) + (dual_z[z, :, cols] - prev_z)
            old = primal[z, :, cols]
            updated = (old + primal_step * divergence + pulled[z, :, cols]) * shrink
            extrapolated[z, :, cols] = 2.0 * updated - old
            primal[z, :, cols] = updated
        return carry

    for iteration in range(ITERS):
        lax.fori_loop(0, planes, plane, 0)
    out_ref[...] = primal[:, :own_rows, :own_cols]


def project(dual_x, dual_y, dual_z, weight):
    scale = jnp.minimum(1.0, weight * lax.rsqrt(dual_x * dual_x + dual_y * dual_y + dual_z * dual_z))
    return (dual_x * scale, dual_y * scale, dual_z * scale)


def per_device(noisy, weight):
    planes, rows_x, rows_y = noisy.shape
    total_x = rows_x * lax.axis_size("gx")
    total_y = rows_y * lax.axis_size("gy")
    start_x = lax.axis_index("gx") * rows_x
    start_y = lax.axis_index("gy") * rows_y
    tail, below, above, width = extend(noisy, weight)
    ext_x = rows_x + 2 * HALO

    local_x = jnp.arange(ext_x, dtype=jnp.int32)
    index_x = jnp.where(local_x >= rows_x + HALO, start_x + local_x - ext_x, start_x + local_x)
    keep_x = (index_x >= 0) & (index_x < total_x - 1)
    local_y = jnp.arange(width, dtype=jnp.int32)
    index_y = jnp.where(local_y >= width - HALO, start_y + local_y - width, start_y + local_y)
    inside_y = (local_y < rows_y + HALO) | (local_y >= width - HALO)
    keep_y = inside_y & (index_y >= 0) & (index_y < total_y - 1)
    step_x = jnp.broadcast_to(jnp.where(keep_x, dual_step, 0.0)[:, None], (ext_x, width)).astype(jnp.float32)
    step_y = jnp.broadcast_to(jnp.where(keep_y, dual_step, 0.0)[None, :], (ext_x, width)).astype(jnp.float32)

    field = jax.ShapeDtypeStruct((planes, ext_x, width), jnp.float32)
    vmem = pl.BlockSpec(memory_space=pltpu.VMEM)
    return pl.pallas_call(
        iterate_kernel,
        out_shape=jax.ShapeDtypeStruct(noisy.shape, jnp.float32),
        in_specs=[vmem] * 9,
        out_specs=vmem,
        scratch_shapes=[pltpu.VMEM(field.shape, jnp.float32)] * 8,
        compiler_params=pltpu.CompilerParams(vmem_limit_bytes=48 * 1024 * 1024),
    )(noisy, weight, tail, *below, *above, step_x, step_y)


def solution(mesh):
    placed = (P(None, "gx", "gy"), P(None, "gx", "gy"))
    return jax.shard_map(
        per_device, mesh=mesh, in_specs=placed, out_specs=P(None, "gx", "gy"), check_vma=False
    )
```

```python
import functools

import jax
import jax.numpy as jnp
from jax import lax
from jax.experimental import pallas as pl
from jax.experimental.pallas import tpu as pltpu
from jax.sharding import PartitionSpec as P

ITERS = 8
HALO = ITERS


dual_step = 0.28
primal_step = 0.28
fidelity = 1.0


def from_offset(value, axis, offset):
    count = lax.axis_size(axis)
    return lax.ppermute(value, axis, [((dest + offset) % count, dest) for dest in range(count)])


def extend(noisy, weight):
    planes, rows, cols = noisy.shape
    width = -(-(cols + 2 * HALO) // 128) * 128
    both = jnp.stack([noisy, weight])
    right = from_offset(both[..., :HALO], "gy", 1)
    left = from_offset(both[..., cols - HALO:], "gy", -1)
    gap = width - cols - 2 * HALO
    filler = jnp.concatenate(
        [jnp.zeros((1, planes, rows, gap), noisy.dtype), jnp.ones((1, planes, rows, gap), noisy.dtype)], 0
    )
    tail = jnp.concatenate([right, filler, left], 3)
    first = jnp.concatenate([both[:, :, :HALO, :], tail[:, :, :HALO, :]], 3)
    last = jnp.concatenate([both[:, :, rows - HALO:, :], tail[:, :, rows - HALO:, :]], 3)
    below = from_offset(first, "gx", 1)
    above = from_offset(last, "gx", -1)
    return tail, below, above, width


LANES = 128


def iterate_kernel(
    own_noisy_ref, own_weight_ref, tail_ref, below_ref, above_ref, step_x_ref, step_y_ref, out_ref,
    noisy_ref, weight_ref, primal, extrapolated, dual_x, dual_y, dual_z, pulled,
):
    planes, rows, width = noisy_ref.shape
    own_rows, own_cols = out_ref.shape[1:]
    halo = below_ref.shape[2]
    blocks = width // LANES
    shrink = 1.0 / (1.0 + primal_step * fidelity)

    def setup(z, carry):
        for field, own_ref, part in ((noisy_ref, own_noisy_ref, 0), (weight_ref, own_weight_ref, 1)):
            field[z, pl.ds(0, own_rows), pl.ds(0, own_cols)] = own_ref[z]
            field[z, pl.ds(0, own_rows), pl.ds(own_cols, width - own_cols)] = tail_ref[part, z]
            field[z, pl.ds(own_rows, halo)] = below_ref[part, z]
            field[z, pl.ds(own_rows + halo, halo)] = above_ref[part, z]
        pulled[z] = primal_step * fidelity * noisy_ref[z]
        return carry

    lax.fori_loop(0, planes, setup, 0)
    lane = lax.broadcasted_iota(jnp.int32, (rows, LANES), 1)
    last_lane = lane == LANES - 1
    first_lane = lane == 0

    def plane(z, carry, first=False):
        start = noisy_ref if first else extrapolated
        begun = noisy_ref if first else primal

        def dual(ref, index, cols):
            return jnp.zeros((rows, LANES), jnp.float32) if first else ref[index, :, cols]

        after = jnp.minimum(z + 1, planes - 1)
        before = jnp.maximum(z - 1, 0)
        step_z = jnp.where(z < planes - 1, dual_step, 0.0)
        turned = [pltpu.roll(start[z, :, pl.ds(block * LANES, LANES)], LANES - 1, 1) for block in range(blocks)]
        for block in range(blocks):
            cols = pl.ds(block * LANES, LANES)
            here = start[z, :, cols]
            next_y = jnp.where(last_lane, turned[(block + 1) % blocks], turned[block])
            next_x = pltpu.roll(here, rows - 1, 0)
            new_x, new_y, new_z = project(
                dual(dual_x, z, cols) + step_x_ref[:, cols] * (next_x - here),
                dual(dual_y, z, cols) + step_y_ref[:, cols] * (next_y - here),
                dual(dual_z, z, cols) + step_z * (start[after, :, cols] - here),
                weight_ref[z, :, cols],
            )
            dual_x[z, :, cols] = new_x
            dual_y[z, :, cols] = new_y
            dual_z[z, :, cols] = new_z
        turned = [pltpu.roll(dual_y[z, :, pl.ds(block * LANES, LANES)], 1, 1) for block in range(blocks)]
        for block in range(blocks):
            cols = pl.ds(block * LANES, LANES)
            new_x = dual_x[z, :, cols]
            new_y = dual_y[z, :, cols]
            prev_y = jnp.where(first_lane, turned[(block - 1) % blocks], turned[block])
            prev_z = jnp.where(z > 0, dual_z[before, :, cols], 0.0)
            divergence = (new_x - pltpu.roll(new_x, 1, 0)) + (new_y - prev_y) + (dual_z[z, :, cols] - prev_z)
            old = begun[z, :, cols]
            updated = (old + primal_step * divergence + pulled[z, :, cols]) * shrink
            extrapolated[z, :, cols] = 2.0 * updated - old
            primal[z, :, cols] = updated
        return carry

    lax.fori_loop(0, planes, functools.partial(plane, first=True), 0)
    for iteration in range(1, ITERS):
        lax.fori_loop(0, planes, plane, 0)
    out_ref[...] = primal[:, :own_rows, :own_cols]


def project(dual_x, dual_y, dual_z, weight):
    scale = jnp.minimum(1.0, weight * lax.rsqrt(dual_x * dual_x + dual_y * dual_y + dual_z * dual_z))
    return (dual_x * scale, dual_y * scale, dual_z * scale)


def per_device(noisy, weight):
    planes, rows_x, rows_y = noisy.shape
    total_x = rows_x * lax.axis_size("gx")
    total_y = rows_y * lax.axis_size("gy")
    start_x = lax.axis_index("gx") * rows_x
    start_y = lax.axis_index("gy") * rows_y
    tail, below, above, width = extend(noisy, weight)
    ext_x = rows_x + 2 * HALO

    local_x = jnp.arange(ext_x, dtype=jnp.int32)
    index_x = jnp.where(local_x >= rows_x + HALO, start_x + local_x - ext_x, start_x + local_x)
    keep_x = (index_x >= 0) & (index_x < total_x - 1)
    local_y = jnp.arange(width, dtype=jnp.int32)
    index_y = jnp.where(local_y >= width - HALO, start_y + local_y - width, start_y + local_y)
    inside_y = (local_y < rows_y + HALO) | (local_y >= width - HALO)
    keep_y = inside_y & (index_y >= 0) & (index_y < total_y - 1)
    step_x = jnp.broadcast_to(jnp.where(keep_x, dual_step, 0.0)[:, None], (ext_x, width)).astype(jnp.float32)
    step_y = jnp.broadcast_to(jnp.where(keep_y, dual_step, 0.0)[None, :], (ext_x, width)).astype(jnp.float32)

    field = jax.ShapeDtypeStruct((planes, ext_x, width), jnp.float32)
    vmem = pl.BlockSpec(memory_space=pltpu.VMEM)
    return pl.pallas_call(
        iterate_kernel,
        out_shape=jax.ShapeDtypeStruct(noisy.shape, jnp.float32),
        in_specs=[vmem] * 7,
        out_specs=vmem,
        scratch_shapes=[pltpu.VMEM(field.shape, jnp.float32)] * 8,
        compiler_params=pltpu.CompilerParams(vmem_limit_bytes=48 * 1024 * 1024),
    )(noisy, weight, tail, below, above, step_x, step_y)


def solution(mesh):
    placed = (P(None, "gx", "gy"), P(None, "gx", "gy"))
    return jax.shard_map(
        per_device, mesh=mesh, in_specs=placed, out_specs=P(None, "gx", "gy"), check_vma=False
    )
```

```python
import functools

import jax
import jax.numpy as jnp
from jax import lax
from jax.experimental import pallas as pl
from jax.experimental.pallas import tpu as pltpu
from jax.sharding import PartitionSpec as P

ITERS = 8
HALO = ITERS


dual_step = 0.28
primal_step = 0.28
fidelity = 1.0


def from_offset(value, axis, offset):
    count = lax.axis_size(axis)
    return lax.ppermute(value, axis, [((dest + offset) % count, dest) for dest in range(count)])


def extend(noisy, weight):
    planes, rows, cols = noisy.shape
    width = -(-(cols + 2 * HALO) // 128) * 128
    both = jnp.stack([noisy, weight])
    right = from_offset(both[..., :HALO], "gy", 1)
    left = from_offset(both[..., cols - HALO:], "gy", -1)
    gap = width - cols - 2 * HALO
    filler = jnp.concatenate(
        [jnp.zeros((1, planes, rows, gap), noisy.dtype), jnp.ones((1, planes, rows, gap), noisy.dtype)], 0
    )
    tail = jnp.concatenate([right, filler, left], 3)
    first = jnp.concatenate([both[:, :, :HALO, :], tail[:, :, :HALO, :]], 3)
    last = jnp.concatenate([both[:, :, rows - HALO:, :], tail[:, :, rows - HALO:, :]], 3)
    below = from_offset(first, "gx", 1)
    above = from_offset(last, "gx", -1)
    return tail, below, above, width


LANES = 128


def iterate_kernel(
    own_noisy_ref, own_weight_ref, tail_ref, below_ref, above_ref, step_x_ref, step_y_ref, out_ref,
    noisy_ref, weight_ref, primal, extrapolated, dual_x, dual_y, dual_z, pulled,
):
    planes, rows, width = noisy_ref.shape
    own_rows, own_cols = out_ref.shape[1:]
    halo = below_ref.shape[2]
    blocks = width // LANES
    shrink = 1.0 / (1.0 + primal_step * fidelity)

    def setup(z, carry):
        for field, own_ref, part in ((noisy_ref, own_noisy_ref, 0), (weight_ref, own_weight_ref, 1)):
            field[z, pl.ds(0, own_rows), pl.ds(0, own_cols)] = own_ref[z]
            field[z, pl.ds(0, own_rows), pl.ds(own_cols, width - own_cols)] = tail_ref[part, z]
            field[z, pl.ds(own_rows, halo)] = below_ref[part, z]
            field[z, pl.ds(own_rows + halo, halo)] = above_ref[part, z]
        pulled[z] = primal_step * fidelity * noisy_ref[z]
        return carry

    lax.fori_loop(0, planes, setup, 0)
    lane = lax.broadcasted_iota(jnp.int32, (rows, LANES), 1)
    last_lane = lane == LANES - 1
    first_lane = lane == 0

    def plane(z, carry, first=False, last=False):
        start = noisy_ref if first else extrapolated
        begun = noisy_ref if first else primal

        def dual(ref, index, cols):
            return jnp.zeros((rows, LANES), jnp.float32) if first else ref[index, :, cols]

        after = jnp.minimum(z + 1, planes - 1)
        before = jnp.maximum(z - 1, 0)
        step_z = jnp.where(z < planes - 1, dual_step, 0.0)
        turned = [pltpu.roll(start[z, :, pl.ds(block * LANES, LANES)], LANES - 1, 1) for block in range(blocks)]
        for block in range(blocks):
            cols = pl.ds(block * LANES, LANES)
            here = start[z, :, cols]
            next_y = jnp.where(last_lane, turned[(block + 1) % blocks], turned[block])
            next_x = pltpu.roll(here, rows - 1, 0)
            new_x, new_y, new_z = project(
                dual(dual_x, z, cols) + step_x_ref[:, cols] * (next_x - here),
                dual(dual_y, z, cols) + step_y_ref[:, cols] * (next_y - here),
                dual(dual_z, z, cols) + step_z * (start[after, :, cols] - here),
                weight_ref[z, :, cols],
            )
            dual_x[z, :, cols] = new_x
            dual_y[z, :, cols] = new_y
            dual_z[z, :, cols] = new_z
        turned = [pltpu.roll(dual_y[z, :, pl.ds(block * LANES, LANES)], 1, 1) for block in range(blocks)]
        for block in range(own_cols // LANES if last else blocks):
            cols = pl.ds(block * LANES, LANES)
            new_x = dual_x[z, :, cols]
            new_y = dual_y[z, :, cols]
            prev_y = jnp.where(first_lane, turned[(block - 1) % blocks], turned[block])
            prev_z = jnp.where(z > 0, dual_z[before, :, cols], 0.0)
            divergence = (new_x - pltpu.roll(new_x, 1, 0)) + (new_y - prev_y) + (dual_z[z, :, cols] - prev_z)
            old = begun[z, :, cols]
            updated = (old + primal_step * divergence + pulled[z, :, cols]) * shrink
            if last:
                out_ref[z, :, cols] = updated[:own_rows]
                continue
            extrapolated[z, :, cols] = 2.0 * updated - old
            primal[z, :, cols] = updated
        return carry

    lax.fori_loop(0, planes, functools.partial(plane, first=True), 0)
    for iteration in range(1, ITERS - 1):
        lax.fori_loop(0, planes, plane, 0)
    lax.fori_loop(0, planes, functools.partial(plane, last=True), 0)


def project(dual_x, dual_y, dual_z, weight):
    scale = jnp.minimum(1.0, weight * lax.rsqrt(dual_x * dual_x + dual_y * dual_y + dual_z * dual_z))
    return (dual_x * scale, dual_y * scale, dual_z * scale)


def per_device(noisy, weight):
    planes, rows_x, rows_y = noisy.shape
    total_x = rows_x * lax.axis_size("gx")
    total_y = rows_y * lax.axis_size("gy")
    start_x = lax.axis_index("gx") * rows_x
    start_y = lax.axis_index("gy") * rows_y
    tail, below, above, width = extend(noisy, weight)
    ext_x = rows_x + 2 * HALO

    local_x = jnp.arange(ext_x, dtype=jnp.int32)
    index_x = jnp.where(local_x >= rows_x + HALO, start_x + local_x - ext_x, start_x + local_x)
    keep_x = (index_x >= 0) & (index_x < total_x - 1)
    local_y = jnp.arange(width, dtype=jnp.int32)
    index_y = jnp.where(local_y >= width - HALO, start_y + local_y - width, start_y + local_y)
    inside_y = (local_y < rows_y + HALO) | (local_y >= width - HALO)
    keep_y = inside_y & (index_y >= 0) & (index_y < total_y - 1)
    step_x = jnp.broadcast_to(jnp.where(keep_x, dual_step, 0.0)[:, None], (ext_x, width)).astype(jnp.float32)
    step_y = jnp.broadcast_to(jnp.where(keep_y, dual_step, 0.0)[None, :], (ext_x, width)).astype(jnp.float32)

    field = jax.ShapeDtypeStruct((planes, ext_x, width), jnp.float32)
    vmem = pl.BlockSpec(memory_space=pltpu.VMEM)
    return pl.pallas_call(
        iterate_kernel,
        out_shape=jax.ShapeDtypeStruct(noisy.shape, jnp.float32),
        in_specs=[vmem] * 7,
        out_specs=vmem,
        scratch_shapes=[pltpu.VMEM(field.shape, jnp.float32)] * 8,
        compiler_params=pltpu.CompilerParams(vmem_limit_bytes=48 * 1024 * 1024),
    )(noisy, weight, tail, below, above, step_x, step_y)


def solution(mesh):
    placed = (P(None, "gx", "gy"), P(None, "gx", "gy"))
    return jax.shard_map(
        per_device, mesh=mesh, in_specs=placed, out_specs=P(None, "gx", "gy"), check_vma=False
    )
```
